256 devices in a mesh: seq: 16 (over x_lo, y, core), chan: 16 (over x_hi, z).
Axes of the slice: x: 4 (x_hi: 2, x_lo: 2; x = x_hi * 2 + x_lo), y: 4, z: 8, core: 2. Of those that a mesh axis runs over, the one named last changes fastest.
Arguments:
- tokens: int32 [4096], P('seq'), may hold values from 0 to 511
- embedding: bfloat16 [512, 4096], P(None, 'chan'), may hold values from -6 to 6
- norm_gain: float32 [4096], replicated, may hold values from 0.5 to 1.5
- in_weight: bfloat16 [4096, 3, 4096], P(None, None, 'chan'), may hold values from -0.09375 to 0.09375
- short_filter: float32 [3, 3, 4096], P(None, None, 'chan'), may hold values from -3 to 3
- decay_rate: float32 [16, 4096], P(None, 'chan'), may hold values from 4.8828125e-06 to 0.025, as said below
- residue: float32 [16, 4096], P(None, 'chan'), may hold values from -0.06 to 0.06
- skip_gain: float32 [4096], P('chan'), may hold values from -4 to 4
- out_weight: bfloat16 [4096, 4096], P('chan'), may hold values from -0.125 to 0.125
Outputs:
- block_out: bfloat16 [4096, 4096], P('seq', 'chan')
The draws below stay inside these ranges and needn't reach their ends.
Inputs may be any that keep to these rules, and one draw needn't show every extreme that they name: `decay_rate`: positive rates.
All inputs are finite; a program needn't handle non-finite values.
Results may differ from the reference program's by a relative error of at most 0.0091.
Values may be sent and summed in bfloat16 or wider, within the bound.
No kernel may reach another device: no remote copies, remote signals or barrier semaphores. Data moves between devices by JAX's collectives and lax.ppermute only.
A program may use at most 128 MiB of HBM per device.

```python
import math
import jax
import jax.numpy as jnp
import numpy as np
from jax import lax

D = 4096
VOCAB = 512
MODES = 16
FEAT = 3
BLK = 128
TOKENS = 4096


def draw_decay_rate(key, part):
    key_slow = jax.random.fold_in(key, 11)
    low_log = math.log(0.02 / TOKENS)
    high_log = math.log(0.025)
    logs = jax.random.uniform(key_slow, (MODES, D), jnp.float32, low_log, high_log)
    return jnp.exp(logs).astype(jnp.float32)


def touch_ends(drawn, stream_key, low, top_value):
    longest = drawn.shape.index(max(drawn.shape))
    spots = []
    for shift in (0, 1):
        where = [jax.random.randint(jax.random.fold_in(stream_key, axis), (), 0, length) for axis, length in enumerate(drawn.shape)]
        where[longest] = (where[longest] + shift) % drawn.shape[longest]
        spots.append(tuple(where))
    return drawn.at[spots[0]].set(low).at[spots[1]].set(top_value)


def raised(drawn, stream_key, source, target, blocks, factor):
    def block_of(axis_at):
        return (jnp.arange(drawn.shape[axis_at]) // (drawn.shape[axis_at] // blocks)).reshape((-1,) + (1,) * (drawn.ndim - 1 - axis_at))

    one_side = jax.random.permutation(stream_key, blocks)[block_of(target)]
    far = (block_of(target) + blocks // 2) % blocks
    return jnp.where((block_of(source) == one_side) | (block_of(source) == far), factor * drawn, drawn)


def levels(own_key, shape, cuts, least, top_value):
    level, own = 1.0, jax.random.fold_in(own_key, 6)
    for dim, blocks in cuts:
        steps = jnp.exp(jax.random.uniform(jax.random.fold_in(own, dim), (blocks,), jnp.float32, least / len(cuts), top_value / len(cuts)))
        level = level * jnp.repeat(steps, shape[dim] // blocks).reshape([-1 if axis == dim else 1 for axis in range(len(shape))])
    return level


def rank_table(amount, slope):
    weights = [(1 << 20) // math.isqrt(rank ** slope) + 1 for rank in range(1, amount + 1)]
    width = 1 + sum(weights) // (1 << 30)
    return np.cumsum(np.array([max(1, weight // width) for weight in weights]))


def ranked(key, dims, count, lean):
    table = rank_table(count, lean)
    pick = jax.random.randint(jax.random.fold_in(key, 1), dims, 0, int(table[count - 1]))
    standing = jnp.searchsorted(jnp.asarray(table, jnp.int32), pick, side="right")
    return jax.random.permutation(jax.random.fold_in(key, 2), count)[standing].astype(jnp.int32)


def noise(key, shape, spread, most, cuts=(), held_as=jnp.bfloat16):
    values = jax.random.normal(key, shape, jnp.float32) * spread
    if len(cuts) > 0:
        values = levels(key, shape, cuts, -0.22, 0.18) * values
    return jnp.clip(values, min=-most, max=most).astype(held_as)


def noise_with(own_key, extent, spread, bound, pieces, heavy, kind=jnp.bfloat16):
    entries = spread * jax.random.normal(own_key, extent, jnp.float32)
    if pieces:
        entries = entries * levels(own_key, extent, pieces, -0.22, 0.18)
    return jnp.clip(raised(entries, jax.random.fold_in(own_key, 3), *heavy), -bound, bound).astype(kind)


def setup_inputs(seed: int = 0) -> dict:
    arg_keys = jax.random.split(jax.random.key(seed), 10)
    tokens = touch_ends(ranked(arg_keys[0], (TOKENS,), VOCAB, 2), jax.random.fold_in(arg_keys[0], 3), 0, VOCAB - 1).astype(jnp.int32)
    embedding = noise(arg_keys[1], (VOCAB, D), 1.0, 6.0, ((1, 16),))
    norm_gain = jnp.clip(1.0 + 0.1 * jax.random.normal(arg_keys[2], (D,), jnp.float32), 0.5, 1.5)
    in_weight = noise(arg_keys[3], (D, 3, D), D ** -0.5, 0.09375, ((2, 16),))
    short_filter = noise(arg_keys[4], (FEAT, 3, D), 0.6, 3.0, ((2, 16),), jnp.float32)
    decay_rate = draw_decay_rate(jax.random.fold_in(arg_keys[9], 71), 0)
    residue = noise(arg_keys[6], (MODES, D), 0.01, 0.06, ((1, 16),), jnp.float32)
    skip_gain = noise(arg_keys[7], (D,), 1.0, 4.0, ((0, 16),), jnp.float32)
    out_weight = noise_with(arg_keys[8], (D, D), D ** -0.5, 0.125, ((0, 16),), (0, 1, 16, 2.0))
    return dict(tokens=tokens, embedding=embedding, norm_gain=norm_gain, in_weight=in_weight, short_filter=short_filter, decay_rate=decay_rate, residue=residue, skip_gain=skip_gain, out_weight=out_weight)


def modal_filter(driven, decay_rate, residue):
    steps_f = jnp.arange(BLK, dtype=jnp.float32)
    lag_table = jnp.arange(BLK)[:, None] - jnp.arange(BLK)[None, :]
    causal = lag_table >= 0
    impulse = lax.optimization_barrier(jnp.sum(residue[:, None, :] * jnp.exp(-decay_rate[:, None, :] * steps_f[None, :, None]), axis=0))
    toeplitz = jnp.where(causal[:, :, None], impulse[jnp.clip(lag_table, 0, BLK - 1)], 0.0)
    w_end = jnp.exp(-decay_rate[:, None, :] * (BLK - 1 - steps_f)[None, :, None])
    r_next = residue[:, None, :] * jnp.exp(-decay_rate[:, None, :] * (steps_f + 1.0)[None, :, None])
    block_decay = jnp.exp(-decay_rate * BLK)
    blocks = driven.reshape(TOKENS // BLK, BLK, D)

    def advance(state, block):
        result = jnp.einsum('ijc,jc->ic', toeplitz, block, precision=lax.Precision.HIGHEST)
        result = result + jnp.einsum('njc,nc->jc', r_next, state, precision=lax.Precision.HIGHEST)
        state = block_decay * state + jnp.einsum('njc,jc->nc', w_end, block, precision=lax.Precision.HIGHEST)
        return (state, result)
    _, results = lax.scan(advance, jnp.zeros((MODES, D), jnp.float32), blocks)
    return results.reshape(TOKENS, D)

def reference(tokens, embedding, norm_gain, in_weight, short_filter, decay_rate, residue, skip_gain, out_weight):
    stream = embedding[tokens]
    stream_f = stream.astype(jnp.float32)
    scale = lax.rsqrt(lax.optimization_barrier(jnp.mean(stream_f * stream_f, axis=1, keepdims=True)) + 1e-06)
    normed = (stream_f * scale * norm_gain[None, :]).astype(jnp.bfloat16)
    proj = jnp.dot(normed, in_weight.reshape(D, 3 * D), preferred_element_type=jnp.float32)
    proj = proj.astype(jnp.bfloat16).reshape(TOKENS, 3, D)
    padded = jnp.concatenate([jnp.zeros((FEAT - 1, 3, D), jnp.bfloat16), proj], axis=0).astype(jnp.float32)
    feat = short_filter[0][None] * padded[FEAT - 1:FEAT - 1 + TOKENS]
    for offset in range(1, FEAT):
        feat = feat + short_filter[offset][None] * padded[FEAT - 1 - offset:FEAT - 1 - offset + TOKENS]
    feat = feat.astype(jnp.bfloat16)
    query = feat[:, 0].astype(jnp.float32)
    driven = feat[:, 1].astype(jnp.float32) * feat[:, 2].astype(jnp.float32)
    long_out = modal_filter(driven, decay_rate, residue) + skip_gain[None, :] * driven
    hidden = (query * long_out).astype(jnp.bfloat16)
    mixed = jnp.dot(hidden, out_weight, preferred_element_type=jnp.float32)
    return (stream_f + mixed).astype(jnp.bfloat16)
```

```python
import jax
import jax.numpy as jnp
from jax import lax
from jax.sharding import PartitionSpec as P

FEAT = 3


def from_behind(value, axis, by):
    devices = lax.axis_size(axis)
    pairs = [(i, i + by) for i in range(devices) if 0 <= i + by < devices]
    return lax.ppermute(value, axis, pairs)


def on_device(
    tokens,
    embedding,
    norm_gain,
    in_weight,
    short_filter,
    decay_rate,
    residue,
    skip_gain,
    out_weight,
):
    token_rows = tokens.shape[0]
    vocab_size = embedding.shape[0]
    channels = embedding.shape[1]
    modes = decay_rate.shape[0]
    seq_devices = lax.axis_size("seq")
    place = lax.axis_index("seq")

    weight_cols = lax.all_to_all(out_weight, "chan", 1, 0, tiled=True)

    one_hot = (tokens[:, None] == jnp.arange(vocab_size, dtype=jnp.int32)[None, :]).astype(
        jnp.bfloat16
    )
    stream = jnp.dot(one_hot, embedding, preferred_element_type=jnp.float32).astype(jnp.bfloat16)
    gathered = lax.all_gather(stream, "chan", axis=1, tiled=True)
    gathered_f = gathered.astype(jnp.float32)
    scale = lax.rsqrt(jnp.mean(gathered_f * gathered_f, axis=1, keepdims=True) + 1e-06)
    normed = (gathered_f * scale * norm_gain[None, :]).astype(jnp.bfloat16)
    proj = jnp.einsum("td,djc->tjc", normed, in_weight, preferred_element_type=jnp.float32).astype(
        jnp.bfloat16
    )
    rim_rows = FEAT - 1
    earlier_rim = from_behind(proj[token_rows - rim_rows :], "seq", 1)
    padded = jnp.concatenate([earlier_rim, proj], axis=0).astype(jnp.float32)
    feat = short_filter[0][None] * padded[rim_rows : rim_rows + token_rows]
    for offset in range(1, FEAT):
        feat = (
            feat
            + short_filter[offset][None]
            * padded[rim_rows - offset : rim_rows - offset + token_rows]
        )
    feat = feat.astype(jnp.bfloat16)
    query = feat[:, 0].astype(jnp.float32)
    driven = feat[:, 1].astype(jnp.float32) * feat[:, 2].astype(jnp.float32)

    pos = jnp.arange(token_rows, dtype=jnp.float32)
    rise = jnp.exp(decay_rate[None] * pos[:, None, None])
    fall = residue[None] * jnp.exp(-decay_rate[None] * pos[:, None, None])
    rows = jnp.arange(token_rows)
    lower = (rows[:, None] >= rows[None, :]).astype(jnp.float32)
    lifted = rise * driven[:, None, :]
    running = jnp.dot(
        lower, lifted.reshape(token_rows, modes * channels), precision=lax.Precision.HIGHEST
    ).reshape(token_rows, modes, channels)
    local = jnp.sum(fall * running, axis=1)
    device_end = jnp.exp(-decay_rate * (token_rows - 1)) * jnp.sum(lifted, axis=0)
    ends = lax.all_gather(device_end, "seq")
    gap = place - 1 - jnp.arange(seq_devices)
    span = jnp.exp(
        -decay_rate[None]
        * (token_rows * jnp.maximum(gap, 0)).astype(jnp.float32)[:, None, None]
    )
    span = jnp.where((gap >= 0)[:, None, None], span, 0.0)
    incoming = jnp.sum(span * ends, axis=0) * jnp.exp(-decay_rate)
    carried = jnp.sum(fall * incoming[None], axis=1)
    long_out = local + carried + skip_gain[None, :] * driven
    hidden = (query * long_out).astype(jnp.bfloat16)
    hidden_all = lax.all_gather(hidden, "chan", axis=1, tiled=True)
    mixed = jnp.dot(hidden_all, weight_cols, preferred_element_type=jnp.float32)
    return (stream.astype(jnp.float32) + mixed).astype(jnp.bfloat16)


def solution(mesh):
    placed = (
        P("seq"),
        P(None, "chan"),
        P(),
        P(None, None, "chan"),
        P(None, None, "chan"),
        P(None, "chan"),
        P(None, "chan"),
        P("chan"),
        P("chan", None),
    )
    return jax.shard_map(
        on_device, mesh=mesh, in_specs=placed, out_specs=P("seq", "chan"), check_vma=False
    )
```

```python
import jax
import jax.numpy as jnp
from jax import lax
from jax.sharding import PartitionSpec as P

FEAT = 3


def from_behind(value, axis, by):
    devices = lax.axis_size(axis)
    pairs = [(i, i + by) for i in range(devices) if 0 <= i + by < devices]
    return lax.ppermute(value, axis, pairs)


def on_device(
    tokens,
    embedding,
    norm_gain,
    in_weight,
    short_filter,
    decay_rate,
    residue,
    skip_gain,
    out_weight,
):
    token_rows = tokens.shape[0]
    vocab_size = embedding.shape[0]
    channels = embedding.shape[1]
    modes = decay_rate.shape[0]
    seq_devices = lax.axis_size("seq")

    one_hot = (tokens[:, None] == jnp.arange(vocab_size, dtype=jnp.int32)[None, :]).astype(
        jnp.bfloat16
    )
    stream = jnp.dot(one_hot, embedding, preferred_element_type=jnp.float32).astype(jnp.bfloat16)
    gathered = lax.all_gather(stream, "chan", axis=1, tiled=True)
    gathered, out_weight = lax.optimization_barrier((gathered, out_weight))
    weight_cols = lax.all_to_all(out_weight, "chan", 1, 0, tiled=True)
    gathered_f = gathered.astype(jnp.float32)
    scale = lax.rsqrt(jnp.mean(gathered_f * gathered_f, axis=1, keepdims=True) + 1e-06)
    normed = (gathered_f * scale * norm_gain[None, :]).astype(jnp.bfloat16)
    proj = jnp.einsum("td,djc->tjc", normed, in_weight, preferred_element_type=jnp.float32).astype(
        jnp.bfloat16
    )
    rim_rows = FEAT - 1
    earlier_rim = from_behind(proj[token_rows - rim_rows :], "seq", 1)
    padded = jnp.concatenate([earlier_rim, proj], axis=0).astype(jnp.float32)
    feat = short_filter[0][None] * padded[rim_rows : rim_rows + token_rows]
    for offset in range(1, FEAT):
        feat = (
            feat
            + short_filter[offset][None]
            * padded[rim_rows - offset : rim_rows - offset + token_rows]
        )
    feat = feat.astype(jnp.bfloat16)
    query = feat[:, 0].astype(jnp.float32)
    driven = feat[:, 1].astype(jnp.float32) * feat[:, 2].astype(jnp.float32)

    pos = jnp.arange(token_rows, dtype=jnp.float32)
    rise = jnp.exp(decay_rate[None] * pos[:, None, None])
    fall = residue[None] * jnp.exp(-decay_rate[None] * pos[:, None, None])
    rows = jnp.arange(token_rows)
    lower = (rows[:, None] >= rows[None, :]).astype(jnp.float32)
    lifted = rise * driven[:, None, :]
    running = jnp.dot(
        lower, lifted.reshape(token_rows, modes * channels), precision=lax.Precision.HIGHEST
    ).reshape(token_rows, modes, channels)
    local = jnp.sum(fall * running, axis=1)
    device_end = jnp.exp(-decay_rate * (token_rows - 1)) * jnp.sum(lifted, axis=0)
    incoming = jnp.zeros_like(device_end)
    for back in range(1, seq_devices):
        received = from_behind(device_end, "seq", back)
        incoming = incoming + jnp.exp(-decay_rate * (token_rows * (back - 1))) * received
    incoming = incoming * jnp.exp(-decay_rate)
    carried = jnp.sum(fall * incoming[None], axis=1)
    long_out = local + carried + skip_gain[None, :] * driven
    hidden = (query * long_out).astype(jnp.bfloat16)
    hidden_all = lax.all_gather(hidden, "chan", axis=1, tiled=True)
    mixed = jnp.dot(hidden_all, weight_cols, preferred_element_type=jnp.float32)
    return (stream.astype(jnp.float32) + mixed).astype(jnp.bfloat16)


def solution(mesh):
    placed = (
        P("seq"),
        P(None, "chan"),
        P(),
        P(None, None, "chan"),
        P(None, None, "chan"),
        P(None, "chan"),
        P(None, "chan"),
        P("chan"),
        P("chan", None),
    )
    return jax.shard_map(
        on_device, mesh=mesh, in_specs=placed, out_specs=P("seq", "chan"), check_vma=False
    )
```

```python
import jax
import jax.numpy as jnp
from jax import lax
from jax.sharding import PartitionSpec as P

FEAT = 3


def from_behind(value, axis, by):
    devices = lax.axis_size(axis)
    pairs = [(i, i + by) for i in range(devices) if 0 <= i + by < devices]
    return lax.ppermute(value, axis, pairs)


def on_device(
    tokens,
    embedding,
    norm_gain,
    in_weight,
    short_filter,
    decay_rate,
    residue,
    skip_gain,
    out_weight,
):
    token_rows = tokens.shape[0]
    vocab_size = embedding.shape[0]
    channels = embedding.shape[1]
    modes = decay_rate.shape[0]
    seq_devices = lax.axis_size("seq")

    one_hot = (tokens[:, None] == jnp.arange(vocab_size, dtype=jnp.int32)[None, :]).astype(
        jnp.bfloat16
    )
    stream = jnp.dot(one_hot, embedding, preferred_element_type=jnp.float32).astype(jnp.bfloat16)
    chan_devices = lax.axis_size("chan")
    gathered = lax.all_to_all(
        jnp.tile(stream, (chan_devices, 1)), "chan", 0, 1, tiled=True
    )
    gathered_f = gathered.astype(jnp.float32)
    scale = lax.rsqrt(jnp.mean(gathered_f * gathered_f, axis=1, keepdims=True) + 1e-06)
    normed = (gathered_f * scale * norm_gain[None, :]).astype(jnp.bfloat16)
    proj = jnp.einsum("td,djc->tjc", normed, in_weight, preferred_element_type=jnp.float32).astype(
        jnp.bfloat16
    )
    rim_rows = FEAT - 1
    earlier_rim = from_behind(proj[token_rows - rim_rows :], "seq", 1)
    padded = jnp.concatenate([earlier_rim, proj], axis=0).astype(jnp.float32)
    feat = short_filter[0][None] * padded[rim_rows : rim_rows + token_rows]
    for offset in range(1, FEAT):
        feat = (
            feat
            + short_filter[offset][None]
            * padded[rim_rows - offset : rim_rows - offset + token_rows]
        )
    feat = feat.astype(jnp.bfloat16)
    query = feat[:, 0].astype(jnp.float32)
    driven = feat[:, 1].astype(jnp.float32) * feat[:, 2].astype(jnp.float32)

    pos = jnp.arange(token_rows, dtype=jnp.float32)
    rise = jnp.exp(decay_rate[None] * pos[:, None, None])
    fall = residue[None] * jnp.exp(-decay_rate[None] * pos[:, None, None])
    rows = jnp.arange(token_rows)
    lower = (rows[:, None] >= rows[None, :]).astype(jnp.float32)
    lifted = rise * driven[:, None, :]
    running = jnp.dot(
        lower, lifted.reshape(token_rows, modes * channels), precision=lax.Precision.HIGHEST
    ).reshape(token_rows, modes, channels)
    local = jnp.sum(fall * running, axis=1)
    device_end = jnp.exp(-decay_rate * (token_rows - 1)) * jnp.sum(lifted, axis=0)
    ends = lax.all_to_all(
        jnp.tile(device_end, (seq_devices, 1)), "seq", 0, 0, tiled=True
    ).reshape(seq_devices, modes, channels)
    gap = lax.axis_index("seq") - 1 - jnp.arange(seq_devices)
    span = jnp.exp(
        -decay_rate[None]
        * (token_rows * jnp.maximum(gap, 0)).astype(jnp.float32)[:, None, None]
    )
    span = jnp.where((gap >= 0)[:, None, None], span, 0.0)
    incoming = jnp.sum(span * ends, axis=0) * jnp.exp(-decay_rate)
    carried = jnp.sum(fall * incoming[None], axis=1)
    long_out = local + carried + skip_gain[None, :] * driven
    hidden = (query * long_out).astype(jnp.bfloat16)
    partial = jnp.dot(hidden, out_weight, preferred_element_type=jnp.float32).astype(jnp.bfloat16)
    parts = lax.all_to_all(partial, "chan", 1, 0, tiled=True)
    mixed = jnp.sum(
        parts.reshape(chan_devices, token_rows, channels).astype(jnp.float32), axis=0
    )
    return (stream.astype(jnp.float32) + mixed).astype(jnp.bfloat16)


def solution(mesh):
    placed = (
        P("seq"),
        P(None, "chan"),
        P(),
        P(None, None, "chan"),
        P(None, None, "chan"),
        P(None, "chan"),
        P(None, "chan"),
        P("chan"),
        P("chan", None),
    )
    return jax.shard_map(
        on_device, mesh=mesh, in_specs=placed, out_specs=P("seq", "chan"), check_vma=False
    )
```

```python
import jax
import jax.numpy as jnp
from jax import lax
from jax.sharding import PartitionSpec as P

FEAT = 3


def from_behind(value, axis, by):
    devices = lax.axis_size(axis)
    pairs = [(i, i + by) for i in range(devices) if 0 <= i + by < devices]
    return lax.ppermute(value, axis, pairs)


def on_device(
    tokens,
    embedding,
    norm_gain,
    in_weight,
    short_filter,
    decay_rate,
    residue,
    skip_gain,
    out_weight,
):
    token_rows = tokens.shape[0]
    vocab_size = embedding.shape[0]
    channels = embedding.shape[1]
    modes = decay_rate.shape[0]
    seq_devices = lax.axis_size("seq")

    one_hot = (tokens[:, None] == jnp.arange(vocab_size, dtype=jnp.int32)[None, :]).astype(
        jnp.bfloat16
    )
    stream = jnp.dot(one_hot, embedding, preferred_element_type=jnp.float32).astype(jnp.bfloat16)
    chan_devices = lax.axis_size("chan")
    half = chan_devices // 2
    partners = [(i, (i + half) % chan_devices) for i in range(chan_devices)]
    groups = [list(range(half)), list(range(half, chan_devices))]
    upper = lax.axis_index("chan") >= half
    other = lax.ppermute(stream, "chan", partners)
    pair = jnp.where(upper, jnp.stack([other, stream]), jnp.stack([stream, other]))
    got = lax.all_to_all(
        jnp.broadcast_to(pair[None], (half,) + pair.shape),
        "chan", 0, 0, axis_index_groups=groups,
    )
    gathered = got.transpose(2, 1, 0, 3).reshape(token_rows, chan_devices * channels)
    gathered_f = gathered.astype(jnp.float32)
    scale = lax.rsqrt(jnp.mean(gathered_f * gathered_f, axis=1, keepdims=True) + 1e-06)
    normed = (gathered_f * scale * norm_gain[None, :]).astype(jnp.bfloat16)
    proj = jnp.einsum("td,djc->tjc", normed, in_weight, preferred_element_type=jnp.float32).astype(
        jnp.bfloat16
    )
    rim_rows = FEAT - 1
    earlier_rim = from_behind(proj[token_rows - rim_rows :], "seq", 1)
    padded = jnp.concatenate([earlier_rim, proj], axis=0).astype(jnp.float32)
    feat = short_filter[0][None] * padded[rim_rows : rim_rows + token_rows]
    for offset in range(1, FEAT):
        feat = (
            feat
            + short_filter[offset][None]
            * padded[rim_rows - offset : rim_rows - offset + token_rows]
        )
    feat = feat.astype(jnp.bfloat16)
    query = feat[:, 0].astype(jnp.float32)
    driven = feat[:, 1].astype(jnp.float32) * feat[:, 2].astype(jnp.float32)

    pos = jnp.arange(token_rows, dtype=jnp.float32)
    rise = jnp.exp(decay_rate[None] * pos[:, None, None])
    fall = residue[None] * jnp.exp(-decay_rate[None] * pos[:, None, None])
    rows = jnp.arange(token_rows)
    lower = (rows[:, None] >= rows[None, :]).astype(jnp.float32)
    lifted = rise * driven[:, None, :]
    running = jnp.dot(
        lower, lifted.reshape(token_rows, modes * channels), precision=lax.Precision.HIGHEST
    ).reshape(token_rows, modes, channels)
    local = jnp.sum(fall * running, axis=1)
    device_end = jnp.exp(-decay_rate * (token_rows - 1)) * jnp.sum(lifted, axis=0)
    ends = lax.all_to_all(
        jnp.tile(device_end, (seq_devices, 1)), "seq", 0, 0, tiled=True
    ).reshape(seq_devices, modes, channels)
    gap = lax.axis_index("seq") - 1 - jnp.arange(seq_devices)
    span = jnp.exp(
        -decay_rate[None]
        * (token_rows * jnp.maximum(gap, 0)).astype(jnp.float32)[:, None, None]
    )
    span = jnp.where((gap >= 0)[:, None, None], span, 0.0)
    incoming = jnp.sum(span * ends, axis=0) * jnp.exp(-decay_rate)
    carried = jnp.sum(fall * incoming[None], axis=1)
    long_out = local + carried + skip_gain[None, :] * driven
    hidden = (query * long_out).astype(jnp.bfloat16)
    partial = jnp.dot(hidden, out_weight, preferred_element_type=jnp.float32).astype(jnp.bfloat16)
    slabs = partial.reshape(token_rows, 2, half, channels).transpose(2, 0, 1, 3)
    parts = lax.all_to_all(slabs, "chan", 0, 0, axis_index_groups=groups)
    group_sum = jnp.sum(parts.astype(jnp.float32), axis=0)
    mine = jnp.where(upper, group_sum[:, 1], group_sum[:, 0])
    theirs = jnp.where(upper, group_sum[:, 0], group_sum[:, 1])
    mixed = mine + lax.ppermute(theirs, "chan", partners)
    return (stream.astype(jnp.float32) + mixed).astype(jnp.bfloat16)


def solution(mesh):
    placed = (
        P("seq"),
        P(None, "chan"),
        P(),
        P(None, None, "chan"),
        P(None, None, "chan"),
        P(None, "chan"),
        P(None, "chan"),
        P("chan"),
        P("chan", None),
    )
    return jax.shard_map(
        on_device, mesh=mesh, in_specs=placed, out_specs=P("seq", "chan"), check_vma=False
    )
```

```python
import jax
import jax.numpy as jnp
from jax import lax
from jax.sharding import PartitionSpec as P

FEAT = 3


def from_behind(value, axis, by):
    devices = lax.axis_size(axis)
    pairs = [(i, i + by) for i in range(devices) if 0 <= i + by < devices]
    return lax.ppermute(value, axis, pairs)


def gather_chan(block, chan_devices):
    ring = chan_devices // 2
    upper = lax.axis_index("chan") >= ring
    where_in_ring = lax.axis_index("chan") % ring

    def along_ring(value, by):
        pairs = [
            (side * ring + z, side * ring + (z + by) % ring)
            for side in range(2)
            for z in range(ring)
        ]
        return lax.ppermute(value, "chan", pairs)

    other = lax.ppermute(block, "chan", [(i, (i + ring) % chan_devices) for i in range(chan_devices)])
    pair = jnp.where(upper, jnp.stack([other, block]), jnp.stack([block, other]))
    ahead, behind = [], []
    fwd, bwd = pair, pair
    for step in range(1, ring // 2 + 1):
        fwd = along_ring(fwd, 1)
        behind.append(fwd)
        if step < ring - ring // 2:
            bwd = along_ring(bwd, -1)
            ahead.append(bwd)
    by_offset = jnp.stack([pair] + ahead + behind[::-1])
    by_place = jnp.roll(by_offset, where_in_ring, axis=0)
    rows = block.shape[0]
    return by_place.transpose(2, 1, 0, 3).reshape(rows, chan_devices * block.shape[1])


def on_device(
    tokens,
    embedding,
    norm_gain,
    in_weight,
    short_filter,
    decay_rate,
    residue,
    skip_gain,
    out_weight,
):
    token_rows = tokens.shape[0]
    vocab_size = embedding.shape[0]
    channels = embedding.shape[1]
    modes = decay_rate.shape[0]
    seq_devices = lax.axis_size("seq")

    one_hot = (tokens[:, None] == jnp.arange(vocab_size, dtype=jnp.int32)[None, :]).astype(
        jnp.bfloat16
    )
    stream = jnp.dot(one_hot, embedding, preferred_element_type=jnp.float32).astype(jnp.bfloat16)
    chan_devices = lax.axis_size("chan")
    gathered = gather_chan(stream, chan_devices)
    gathered_f = gathered.astype(jnp.float32)
    scale = lax.rsqrt(jnp.mean(gathered_f * gathered_f, axis=1, keepdims=True) + 1e-06)
    normed = (gathered_f * scale * norm_gain[None, :]).astype(jnp.bfloat16)
    proj = jnp.einsum("td,djc->tjc", normed, in_weight, preferred_element_type=jnp.float32).astype(
        jnp.bfloat16
    )
    rim_rows = FEAT - 1
    earlier_rim = from_behind(proj[token_rows - rim_rows :], "seq", 1)
    padded = jnp.concatenate([earlier_rim, proj], axis=0).astype(jnp.float32)
    feat = short_filter[0][None] * padded[rim_rows : rim_rows + token_rows]
    for offset in range(1, FEAT):
        feat = (
            feat
            + short_filter[offset][None]
            * padded[rim_rows - offset : rim_rows - offset + token_rows]
        )
    feat = feat.astype(jnp.bfloat16)
    query = feat[:, 0].astype(jnp.float32)
    driven = feat[:, 1].astype(jnp.float32) * feat[:, 2].astype(jnp.float32)

    pos = jnp.arange(token_rows, dtype=jnp.float32)
    rise = jnp.exp(decay_rate[None] * pos[:, None, None])
    fall = residue[None] * jnp.exp(-decay_rate[None] * pos[:, None, None])
    rows = jnp.arange(token_rows)
    lower = (rows[:, None] >= rows[None, :]).astype(jnp.float32)
    lifted = rise * driven[:, None, :]
    running = jnp.dot(
        lower, lifted.reshape(token_rows, modes * channels), precision=lax.Precision.HIGHEST
    ).reshape(token_rows, modes, channels)
    local = jnp.sum(fall * running, axis=1)
    device_end = jnp.exp(-decay_rate * (token_rows - 1)) * jnp.sum(lifted, axis=0)
    ends = lax.all_to_all(
        jnp.tile(device_end, (seq_devices, 1)), "seq", 0, 0, tiled=True
    ).reshape(seq_devices, modes, channels)
    gap = lax.axis_index("seq") - 1 - jnp.arange(seq_devices)
    span = jnp.exp(
        -decay_rate[None]
        * (token_rows * jnp.maximum(gap, 0)).astype(jnp.float32)[:, None, None]
    )
    span = jnp.where((gap >= 0)[:, None, None], span, 0.0)
    incoming = jnp.sum(span * ends, axis=0) * jnp.exp(-decay_rate)
    carried = jnp.sum(fall * incoming[None], axis=1)
    long_out = local + carried + skip_gain[None, :] * driven
    hidden = (query * long_out).astype(jnp.bfloat16)
    partial = jnp.dot(hidden, out_weight, preferred_element_type=jnp.float32).astype(jnp.bfloat16)
    parts = lax.all_to_all(partial, "chan", 1, 0, tiled=True)
    mixed = jnp.sum(
        parts.reshape(chan_devices, token_rows, channels).astype(jnp.float32), axis=0
    )
    return (stream.astype(jnp.float32) + mixed).astype(jnp.bfloat16)


def solution(mesh):
    placed = (
        P("seq"),
        P(None, "chan"),
        P(),
        P(None, None, "chan"),
        P(None, None, "chan"),
        P(None, "chan"),
        P(None, "chan"),
        P("chan"),
        P("chan", None),
    )
    return jax.shard_map(
        on_device, mesh=mesh, in_specs=placed, out_specs=P("seq", "chan"), check_vma=False
    )
```

```python
import jax
import jax.numpy as jnp
from jax import lax
from jax.sharding import PartitionSpec as P

FEAT = 3


def from_behind(value, axis, by):
    devices = lax.axis_size(axis)
    pairs = [(i, i + by) for i in range(devices) if 0 <= i + by < devices]
    return lax.ppermute(value, axis, pairs)


def gather_chan(block, chan_devices):
    ring = chan_devices // 2
    upper = lax.axis_index("chan") >= ring
    where_in_ring = lax.axis_index("chan") % ring

    def along_ring(value, by):
        pairs = [
            (side * ring + z, side * ring + (z + by) % ring)
            for side in range(2)
            for z in range(ring)
        ]
        return lax.ppermute(value, "chan", pairs)

    other = lax.ppermute(block, "chan", [(i, (i + ring) % chan_devices) for i in range(chan_devices)])
    pair = jnp.where(upper, jnp.stack([other, block]), jnp.stack([block, other]))
    ahead, behind = [], []
    fwd, bwd = pair, pair
    for step in range(1, ring // 2 + 1):
        fwd = along_ring(fwd, 1)
        behind.append(fwd)
        if step < ring - ring // 2:
            bwd = along_ring(bwd, -1)
            ahead.append(bwd)
    by_offset = jnp.stack([pair] + ahead + behind[::-1])
    by_place = jnp.roll(by_offset, where_in_ring, axis=0)
    rows = block.shape[0]
    return by_place.transpose(2, 1, 0, 3).reshape(rows, chan_devices * block.shape[1])


def reduce_chan(partial, chan_devices, width):
    ring = chan_devices // 2
    upper = lax.axis_index("chan") >= ring
    where_in_ring = lax.axis_index("chan") % ring
    rows = partial.shape[0]
    slabs = partial.reshape(rows, 2, ring, width)

    def along_ring(value, by):
        pairs = [
            (side * ring + z, side * ring + (z + by) % ring)
            for side in range(2)
            for z in range(ring)
        ]
        return lax.ppermute(value, "chan", pairs)

    def slab(offset):
        return lax.dynamic_index_in_dim(slabs, (where_in_ring + offset) % ring, 2, False)

    forward_steps = ring // 2
    backward_steps = ring - 1 - forward_steps
    fwd = slab(forward_steps)
    for step in range(1, forward_steps + 1):
        fwd = along_ring(fwd.astype(jnp.bfloat16), 1).astype(jnp.float32)
        if step < forward_steps:
            fwd = fwd + slab(forward_steps - step)
    total = slab(0) + fwd
    if backward_steps > 0:
        bwd = slab(-backward_steps)
        for step in range(1, backward_steps + 1):
            bwd = along_ring(bwd.astype(jnp.bfloat16), -1).astype(jnp.float32)
            if step < backward_steps:
                bwd = bwd + slab(step - backward_steps)
        total = total + bwd
    mine = jnp.where(upper, total[:, 1], total[:, 0])
    theirs = jnp.where(upper, total[:, 0], total[:, 1])
    partners = [(i, (i + ring) % chan_devices) for i in range(chan_devices)]
    return mine + lax.ppermute(theirs, "chan", partners)


def on_device(
    tokens,
    embedding,
    norm_gain,
    in_weight,
    short_filter,
    decay_rate,
    residue,
    skip_gain,
    out_weight,
):
    token_rows = tokens.shape[0]
    vocab_size = embedding.shape[0]
    channels = embedding.shape[1]
    modes = decay_rate.shape[0]
    seq_devices = lax.axis_size("seq")

    one_hot = (tokens[:, None] == jnp.arange(vocab_size, dtype=jnp.int32)[None, :]).astype(
        jnp.bfloat16
    )
    stream = jnp.dot(one_hot, embedding, preferred_element_type=jnp.float32).astype(jnp.bfloat16)
    chan_devices = lax.axis_size("chan")
    gathered = gather_chan(stream, chan_devices)
    gathered_f = gathered.astype(jnp.float32)
    scale = lax.rsqrt(jnp.mean(gathered_f * gathered_f, axis=1, keepdims=True) + 1e-06)
    normed = (gathered_f * scale * norm_gain[None, :]).astype(jnp.bfloat16)
    proj = jnp.einsum("td,djc->tjc", normed, in_weight, preferred_element_type=jnp.float32).astype(
        jnp.bfloat16
    )
    rim_rows = FEAT - 1
    earlier_rim = from_behind(proj[token_rows - rim_rows :], "seq", 1)
    padded = jnp.concatenate([earlier_rim, proj], axis=0).astype(jnp.float32)
    feat = short_filter[0][None] * padded[rim_rows : rim_rows + token_rows]
    for offset in range(1, FEAT):
        feat = (
            feat
            + short_filter[offset][None]
            * padded[rim_rows - offset : rim_rows - offset + token_rows]
        )
    feat = feat.astype(jnp.bfloat16)
    query = feat[:, 0].astype(jnp.float32)
    driven = feat[:, 1].astype(jnp.float32) * feat[:, 2].astype(jnp.float32)

    pos = jnp.arange(token_rows, dtype=jnp.float32)
    rise = jnp.exp(decay_rate[None] * pos[:, None, None])
    fall = residue[None] * jnp.exp(-decay_rate[None] * pos[:, None, None])
    rows = jnp.arange(token_rows)
    lower = (rows[:, None] >= rows[None, :]).astype(jnp.float32)
    lifted = rise * driven[:, None, :]
    running = jnp.dot(
        lower, lifted.reshape(token_rows, modes * channels), precision=lax.Precision.HIGHEST
    ).reshape(token_rows, modes, channels)
    local = jnp.sum(fall * running, axis=1)
    device_end = jnp.exp(-decay_rate * (token_rows - 1)) * jnp.sum(lifted, axis=0)
    ends = lax.all_to_all(
        jnp.tile(device_end, (seq_devices, 1)), "seq", 0, 0, tiled=True
    ).reshape(seq_devices, modes, channels)
    gap = lax.axis_index("seq") - 1 - jnp.arange(seq_devices)
    span = jnp.exp(
        -decay_rate[None]
        * (token_rows * jnp.maximum(gap, 0)).astype(jnp.float32)[:, None, None]
    )
    span = jnp.where((gap >= 0)[:, None, None], span, 0.0)
    incoming = jnp.sum(span * ends, axis=0) * jnp.exp(-decay_rate)
    carried = jnp.sum(fall * incoming[None], axis=1)
    long_out = local + carried + skip_gain[None, :] * driven
    hidden = (query * long_out).astype(jnp.bfloat16)
    partial = jnp.dot(hidden, out_weight, preferred_element_type=jnp.float32)
    mixed = reduce_chan(partial, chan_devices, channels)
    return (stream.astype(jnp.float32) + mixed).astype(jnp.bfloat16)


def solution(mesh):
    placed = (
        P("seq"),
        P(None, "chan"),
        P(),
        P(None, None, "chan"),
        P(None, None, "chan"),
        P(None, "chan"),
        P(None, "chan"),
        P("chan"),
        P("chan", None),
    )
    return jax.shard_map(
        on_device, mesh=mesh, in_specs=placed, out_specs=P("seq", "chan"), check_vma=False
    )
```

```python
import jax
import jax.numpy as jnp
from jax import lax
from jax.sharding import PartitionSpec as P

FEAT = 3


def from_behind(value, axis, by):
    devices = lax.axis_size(axis)
    pairs = [(i, i + by) for i in range(devices) if 0 <= i + by < devices]
    return lax.ppermute(value, axis, pairs)


def gather_chan(block, chan_devices):
    ring = chan_devices // 2
    upper = lax.axis_index("chan") >= ring
    where_in_ring = lax.axis_index("chan") % ring

    def along_ring(value, by):
        pairs = [
            (side * ring + z, side * ring + (z + by) % ring)
            for side in range(2)
            for z in range(ring)
        ]
        return lax.ppermute(value, "chan", pairs)

    other = lax.ppermute(block, "chan", [(i, (i + ring) % chan_devices) for i in range(chan_devices)])
    pair = jnp.where(upper, jnp.stack([other, block]), jnp.stack([block, other]))
    ahead, behind = [], []
    fwd, bwd = pair, pair
    for step in range(1, ring // 2 + 1):
        fwd = along_ring(fwd, 1)
        behind.append(fwd)
        if step < ring - ring // 2:
            bwd = along_ring(bwd, -1)
            ahead.append(bwd)
    by_offset = jnp.stack([pair] + ahead + behind[::-1])
    by_place = jnp.roll(by_offset, where_in_ring, axis=0)
    rows = block.shape[0]
    return by_place.transpose(2, 1, 0, 3).reshape(rows, chan_devices * block.shape[1])


def reduce_chan(hidden, out_weight, chan_devices, width):
    ring = chan_devices // 2
    upper = lax.axis_index("chan") >= ring
    where_in_ring = lax.axis_index("chan") % ring
    rows = hidden.shape[0]
    rolled = jnp.roll(
        out_weight.reshape(out_weight.shape[0], 2, ring, width), -where_in_ring, axis=2
    ).reshape(out_weight.shape)
    slabs = jnp.dot(hidden, rolled, preferred_element_type=jnp.float32).reshape(
        rows, 2, ring, width
    )

    def along_ring(value, by):
        pairs = [
            (side * ring + z, side * ring + (z + by) % ring)
            for side in range(2)
            for z in range(ring)
        ]
        return lax.ppermute(value, "chan", pairs)

    def slab(offset):
        return slabs[:, :, offset % ring]

    forward_steps = ring // 2
    backward_steps = ring - 1 - forward_steps
    fwd = slab(forward_steps)
    for step in range(1, forward_steps + 1):
        fwd = along_ring(fwd.astype(jnp.bfloat16), 1).astype(jnp.float32)
        if step < forward_steps:
            fwd = fwd + slab(forward_steps - step)
    total = slab(0) + fwd
    if backward_steps > 0:
        bwd = slab(-backward_steps)
        for step in range(1, backward_steps + 1):
            bwd = along_ring(bwd.astype(jnp.bfloat16), -1).astype(jnp.float32)
            if step < backward_steps:
                bwd = bwd + slab(step - backward_steps)
        total = total + bwd
    mine = jnp.where(upper, total[:, 1], total[:, 0])
    theirs = jnp.where(upper, total[:, 0], total[:, 1])
    partners = [(i, (i + ring) % chan_devices) for i in range(chan_devices)]
    return mine + lax.ppermute(theirs, "chan", partners)


def on_device(
    tokens,
    embedding,
    norm_gain,
    in_weight,
    short_filter,
    decay_rate,
    residue,
    skip_gain,
    out_weight,
):
    token_rows = tokens.shape[0]
    vocab_size = embedding.shape[0]
    channels = embedding.shape[1]
    modes = decay_rate.shape[0]
    seq_devices = lax.axis_size("seq")

    one_hot = (tokens[:, None] == jnp.arange(vocab_size, dtype=jnp.int32)[None, :]).astype(
        jnp.bfloat16
    )
    stream = jnp.dot(one_hot, embedding, preferred_element_type=jnp.float32).astype(jnp.bfloat16)
    chan_devices = lax.axis_size("chan")
    gathered = gather_chan(stream, chan_devices)
    gathered_f = gathered.astype(jnp.float32)
    scale = lax.rsqrt(jnp.mean(gathered_f * gathered_f, axis=1, keepdims=True) + 1e-06)
    normed = (gathered_f * scale * norm_gain[None, :]).astype(jnp.bfloat16)
    proj = jnp.einsum("td,djc->tjc", normed, in_weight, preferred_element_type=jnp.float32).astype(
        jnp.bfloat16
    )
    rim_rows = FEAT - 1
    earlier_rim = from_behind(proj[token_rows - rim_rows :], "seq", 1)
    padded = jnp.concatenate([earlier_rim, proj], axis=0).astype(jnp.float32)
    feat = short_filter[0][None] * padded[rim_rows : rim_rows + token_rows]
    for offset in range(1, FEAT):
        feat = (
            feat
            + short_filter[offset][None]
            * padded[rim_rows - offset : rim_rows - offset + token_rows]
        )
    feat = feat.astype(jnp.bfloat16)
    query = feat[:, 0].astype(jnp.float32)
    driven = feat[:, 1].astype(jnp.float32) * feat[:, 2].astype(jnp.float32)

    pos = jnp.arange(token_rows, dtype=jnp.float32)
    rise = jnp.exp(decay_rate[None] * pos[:, None, None])
    fall = residue[None] * jnp.exp(-decay_rate[None] * pos[:, None, None])
    rows = jnp.arange(token_rows)
    lower = (rows[:, None] >= rows[None, :]).astype(jnp.float32)
    lifted = rise * driven[:, None, :]
    running = jnp.dot(
        lower, lifted.reshape(token_rows, modes * channels), precision=lax.Precision.HIGHEST
    ).reshape(token_rows, modes, channels)
    local = jnp.sum(fall * running, axis=1)
    device_end = jnp.exp(-decay_rate * (token_rows - 1)) * jnp.sum(lifted, axis=0)
    ends = lax.all_to_all(
        jnp.tile(device_end, (seq_devices, 1)), "seq", 0, 0, tiled=True
    ).reshape(seq_devices, modes, channels)
    gap = lax.axis_index("seq") - 1 - jnp.arange(seq_devices)
    span = jnp.exp(
        -decay_rate[None]
        * (token_rows * jnp.maximum(gap, 0)).astype(jnp.float32)[:, None, None]
    )
    span = jnp.where((gap >= 0)[:, None, None], span, 0.0)
    incoming = jnp.sum(span * ends, axis=0) * jnp.exp(-decay_rate)
    carried = jnp.sum(fall * incoming[None], axis=1)
    long_out = local + carried + skip_gain[None, :] * driven
    hidden = (query * long_out).astype(jnp.bfloat16)
    mixed = reduce_chan(hidden, out_weight, chan_devices, channels)
    return (stream.astype(jnp.float32) + mixed).astype(jnp.bfloat16)


def solution(mesh):
    placed = (
        P("seq"),
        P(None, "chan"),
        P(),
        P(None, None, "chan"),
        P(None, None, "chan"),
        P(None, "chan"),
        P(None, "chan"),
        P("chan"),
        P("chan", None),
    )
    return jax.shard_map(
        on_device, mesh=mesh, in_specs=placed, out_specs=P("seq", "chan"), check_vma=False
    )
```

```python
import jax
import jax.numpy as jnp
from jax import lax
from jax.sharding import PartitionSpec as P

FEAT = 3


def from_behind(value, axis, by):
    devices = lax.axis_size(axis)
    pairs = [(i, i + by) for i in range(devices) if 0 <= i + by < devices]
    return lax.ppermute(value, axis, pairs)


def gather_chan(block, chan_devices):
    ring = chan_devices // 2
    upper = lax.axis_index("chan") >= ring
    where_in_ring = lax.axis_index("chan") % ring

    def along_ring(value, by):
        pairs = [
            (side * ring + z, side * ring + (z + by) % ring)
            for side in range(2)
            for z in range(ring)
        ]
        return lax.ppermute(value, "chan", pairs)

    other = lax.ppermute(block, "chan", [(i, (i + ring) % chan_devices) for i in range(chan_devices)])
    pair = jnp.where(upper, jnp.stack([other, block]), jnp.stack([block, other]))
    ahead, behind = [], []
    fwd, bwd = pair, pair
    for step in range(1, ring // 2 + 1):
        fwd = along_ring(fwd, 1)
        behind.append(fwd)
        if step < ring - ring // 2:
            bwd = along_ring(bwd, -1)
            ahead.append(bwd)
    by_offset = jnp.stack([pair] + ahead + behind[::-1])
    by_place = jnp.roll(by_offset, where_in_ring, axis=0)
    rows = block.shape[0]
    return by_place.transpose(2, 1, 0, 3).reshape(rows, chan_devices * block.shape[1])


def reduce_chan(hidden, out_weight, chan_devices, width):
    ring = chan_devices // 2
    upper = lax.axis_index("chan") >= ring
    where_in_ring = lax.axis_index("chan") % ring
    rows = hidden.shape[0]
    rolled = jnp.roll(
        out_weight.reshape(out_weight.shape[0], 2, ring, width), -where_in_ring, axis=2
    ).reshape(out_weight.shape)
    slabs = jnp.dot(hidden, rolled, preferred_element_type=jnp.float32).reshape(
        rows, 2, ring, width
    )

    def along_ring(value, by):
        pairs = [
            (side * ring + z, side * ring + (z + by) % ring)
            for side in range(2)
            for z in range(ring)
        ]
        return lax.ppermute(value, "chan", pairs)

    def slab(offset):
        return slabs[:, :, offset % ring]

    forward_steps = ring // 2
    backward_steps = ring - 1 - forward_steps
    fwd = slab(forward_steps)
    bwd = slab(-backward_steps)
    for step in range(1, forward_steps + 1):
        fwd = along_ring(fwd.astype(jnp.bfloat16), 1).astype(jnp.float32)
        if step <= backward_steps:
            bwd = along_ring(bwd.astype(jnp.bfloat16), -1).astype(jnp.float32)
        if step < forward_steps:
            fwd = fwd + slab(forward_steps - step)
        if step < backward_steps:
            bwd = bwd + slab(step - backward_steps)
    total = slab(0) + fwd
    if backward_steps > 0:
        total = total + bwd
    mine = jnp.where(upper, total[:, 1], total[:, 0])
    theirs = jnp.where(upper, total[:, 0], total[:, 1])
    partners = [(i, (i + ring) % chan_devices) for i in range(chan_devices)]
    return mine + lax.ppermute(theirs, "chan", partners)


def on_device(
    tokens,
    embedding,
    norm_gain,
    in_weight,
    short_filter,
    decay_rate,
    residue,
    skip_gain,
    out_weight,
):
    token_rows = tokens.shape[0]
    vocab_size = embedding.shape[0]
    channels = embedding.shape[1]
    modes = decay_rate.shape[0]
    seq_devices = lax.axis_size("seq")

    one_hot = (tokens[:, None] == jnp.arange(vocab_size, dtype=jnp.int32)[None, :]).astype(
        jnp.bfloat16
    )
    stream = jnp.dot(one_hot, embedding, preferred_element_type=jnp.float32).astype(jnp.bfloat16)
    chan_devices = lax.axis_size("chan")
    gathered = gather_chan(stream, chan_devices)
    gathered_f = gathered.astype(jnp.float32)
    scale = lax.rsqrt(jnp.mean(gathered_f * gathered_f, axis=1, keepdims=True) + 1e-06)
    normed = (gathered_f * scale * norm_gain[None, :]).astype(jnp.bfloat16)
    proj = jnp.einsum("td,djc->tjc", normed, in_weight, preferred_element_type=jnp.float32).astype(
        jnp.bfloat16
    )
    rim_rows = FEAT - 1
    earlier_rim = from_behind(proj[token_rows - rim_rows :], "seq", 1)
    padded = jnp.concatenate([earlier_rim, proj], axis=0).astype(jnp.float32)
    feat = short_filter[0][None] * padded[rim_rows : rim_rows + token_rows]
    for offset in range(1, FEAT):
        feat = (
            feat
            + short_filter[offset][None]
            * padded[rim_rows - offset : rim_rows - offset + token_rows]
        )
    feat = feat.astype(jnp.bfloat16)
    query = feat[:, 0].astype(jnp.float32)
    driven = feat[:, 1].astype(jnp.float32) * feat[:, 2].astype(jnp.float32)

    pos = jnp.arange(token_rows, dtype=jnp.float32)
    rise = jnp.exp(decay_rate[None] * pos[:, None, None])
    fall = residue[None] * jnp.exp(-decay_rate[None] * pos[:, None, None])
    rows = jnp.arange(token_rows)
    lower = (rows[:, None] >= rows[None, :]).astype(jnp.float32)
    lifted = rise * driven[:, None, :]
    running = jnp.dot(
        lower, lifted.reshape(token_rows, modes * channels), precision=lax.Precision.HIGHEST
    ).reshape(token_rows, modes, channels)
    local = jnp.sum(fall * running, axis=1)
    device_end = jnp.exp(-decay_rate * (token_rows - 1)) * jnp.sum(lifted, axis=0)
    held_weight, device_end = lax.optimization_barrier((out_weight, device_end))
    ends = lax.all_to_all(
        jnp.tile(device_end, (seq_devices, 1)), "seq", 0, 0, tiled=True
    ).reshape(seq_devices, modes, channels)
    gap = lax.axis_index("seq") - 1 - jnp.arange(seq_devices)
    span = jnp.exp(
        -decay_rate[None]
        * (token_rows * jnp.maximum(gap, 0)).astype(jnp.float32)[:, None, None]
    )
    span = jnp.where((gap >= 0)[:, None, None], span, 0.0)
    incoming = jnp.sum(span * ends, axis=0) * jnp.exp(-decay_rate)
    carried = jnp.sum(fall * incoming[None], axis=1)
    long_out = local + carried + skip_gain[None, :] * driven
    hidden = (query * long_out).astype(jnp.bfloat16)
    mixed = reduce_chan(hidden, held_weight, chan_devices, channels)
    return (stream.astype(jnp.float32) + mixed).astype(jnp.bfloat16)


def solution(mesh):
    placed = (
        P("seq"),
        P(None, "chan"),
        P(),
        P(None, None, "chan"),
        P(None, None, "chan"),
        P(None, "chan"),
        P(None, "chan"),
        P("chan"),
        P("chan", None),
    )
    return jax.shard_map(
        on_device, mesh=mesh, in_specs=placed, out_specs=P("seq", "chan"), check_vma=False
    )
```

```python
import jax
import jax.numpy as jnp
from jax import lax
from jax.sharding import PartitionSpec as P

FEAT = 3


def from_behind(value, axis, by):
    devices = lax.axis_size(axis)
    pairs = [(i, i + by) for i in range(devices) if 0 <= i + by < devices]
    return lax.ppermute(value, axis, pairs)


def gather_chan(block, chan_devices):
    ring = chan_devices // 2
    upper = lax.axis_index("chan") >= ring
    where_in_ring = lax.axis_index("chan") % ring

    def along_ring(value, by):
        pairs = [
            (side * ring + z, side * ring + (z + by) % ring)
            for side in range(2)
            for z in range(ring)
        ]
        return lax.ppermute(value, "chan", pairs)

    def around(value):
        ahead, behind = [], []
        fwd, bwd = value, value
        for step in range(1, ring // 2 + 1):
            fwd = along_ring(fwd, 1)
            behind.append(fwd)
            if step < ring - ring // 2:
                bwd = along_ring(bwd, -1)
                ahead.append(bwd)
        by_offset = jnp.stack([value] + ahead + behind[::-1])
        return jnp.roll(by_offset, where_in_ring, axis=0)

    other = lax.ppermute(block, "chan", [(i, (i + ring) % chan_devices) for i in range(chan_devices)])
    own_side = around(block)
    other_side = around(other)
    by_place = jnp.where(
        upper, jnp.stack([other_side, own_side]), jnp.stack([own_side, other_side])
    )
    rows = block.shape[0]
    return by_place.transpose(2, 0, 1, 3).reshape(rows, chan_devices * block.shape[1])


def reduce_chan(hidden, out_weight, chan_devices, width):
    ring = chan_devices // 2
    upper = lax.axis_index("chan") >= ring
    where_in_ring = lax.axis_index("chan") % ring
    rows = hidden.shape[0]
    rolled = jnp.roll(
        out_weight.reshape(out_weight.shape[0], 2, ring, width), -where_in_ring, axis=2
    ).reshape(out_weight.shape)
    slabs = jnp.dot(hidden, rolled, preferred_element_type=jnp.float32).reshape(
        rows, 2, ring, width
    )

    def along_ring(value, by):
        pairs = [
            (side * ring + z, side * ring + (z + by) % ring)
            for side in range(2)
            for z in range(ring)
        ]
        return lax.ppermute(value, "chan", pairs)

    pieces = lax.optimization_barrier(tuple(slabs[:, :, o] for o in range(ring)))

    def slab(offset):
        return pieces[offset % ring]

    forward_steps = ring // 2
    backward_steps = ring - 1 - forward_steps
    fwd = slab(forward_steps)
    bwd = slab(-backward_steps)
    for step in range(1, forward_steps + 1):
        fwd = along_ring(fwd.astype(jnp.bfloat16), 1).astype(jnp.float32)
        if step <= backward_steps:
            bwd = along_ring(bwd.astype(jnp.bfloat16), -1).astype(jnp.float32)
        if step < forward_steps:
            fwd = fwd + slab(forward_steps - step)
        if step < backward_steps:
            bwd = bwd + slab(step - backward_steps)
    total = slab(0) + fwd
    if backward_steps > 0:
        total = total + bwd
    mine = jnp.where(upper, total[:, 1], total[:, 0])
    theirs = jnp.where(upper, total[:, 0], total[:, 1])
    partners = [(i, (i + ring) % chan_devices) for i in range(chan_devices)]
    return mine + lax.ppermute(theirs, "chan", partners)


def on_device(
    tokens,
    embedding,
    norm_gain,
    in_weight,
    short_filter,
    decay_rate,
    residue,
    skip_gain,
    out_weight,
):
    token_rows = tokens.shape[0]
    vocab_size = embedding.shape[0]
    channels = embedding.shape[1]
    modes = decay_rate.shape[0]
    seq_devices = lax.axis_size("seq")

    one_hot = (tokens[:, None] == jnp.arange(vocab_size, dtype=jnp.int32)[None, :]).astype(
        jnp.bfloat16
    )
    stream = jnp.dot(one_hot, embedding, preferred_element_type=jnp.float32).astype(jnp.bfloat16)
    chan_devices = lax.axis_size("chan")
    gathered = gather_chan(stream, chan_devices)
    gathered_f = gathered.astype(jnp.float32)
    scale = lax.rsqrt(jnp.mean(gathered_f * gathered_f, axis=1, keepdims=True) + 1e-06)
    normed = (gathered_f * scale * norm_gain[None, :]).astype(jnp.bfloat16)
    proj = jnp.einsum("td,djc->tjc", normed, in_weight, preferred_element_type=jnp.float32).astype(
        jnp.bfloat16
    )
    rim_rows = FEAT - 1
    earlier_rim = from_behind(proj[token_rows - rim_rows :], "seq", 1)
    padded = jnp.concatenate([earlier_rim, proj], axis=0).astype(jnp.float32)
    feat = short_filter[0][None] * padded[rim_rows : rim_rows + token_rows]
    for offset in range(1, FEAT):
        feat = (
            feat
            + short_filter[offset][None]
            * padded[rim_rows - offset : rim_rows - offset + token_rows]
        )
    feat = feat.astype(jnp.bfloat16)
    query = feat[:, 0].astype(jnp.float32)
    driven = feat[:, 1].astype(jnp.float32) * feat[:, 2].astype(jnp.float32)

    pos = jnp.arange(token_rows, dtype=jnp.float32)
    rise = jnp.exp(decay_rate[None] * pos[:, None, None])
    fall = residue[None] * jnp.exp(-decay_rate[None] * pos[:, None, None])
    rows = jnp.arange(token_rows)
    lower = (rows[:, None] >= rows[None, :]).astype(jnp.float32)
    lifted = rise * driven[:, None, :]
    running = jnp.dot(
        lower, lifted.reshape(token_rows, modes * channels), precision=lax.Precision.HIGHEST
    ).reshape(token_rows, modes, channels)
    local = jnp.sum(fall * running, axis=1)
    device_end = jnp.exp(-decay_rate * (token_rows - 1)) * jnp.sum(lifted, axis=0)
    held_weight, device_end = lax.optimization_barrier((out_weight, device_end))
    ends = lax.all_to_all(
        jnp.tile(device_end, (seq_devices, 1)), "seq", 0, 0, tiled=True
    ).reshape(seq_devices, modes, channels)
    gap = lax.axis_index("seq") - 1 - jnp.arange(seq_devices)
    span = jnp.exp(
        -decay_rate[None]
        * (token_rows * jnp.maximum(gap, 0)).astype(jnp.float32)[:, None, None]
    )
    span = jnp.where((gap >= 0)[:, None, None], span, 0.0)
    incoming = jnp.sum(span * ends, axis=0) * jnp.exp(-decay_rate)
    carried = jnp.sum(fall * incoming[None], axis=1)
    long_out = local + carried + skip_gain[None, :] * driven
    hidden = (query * long_out).astype(jnp.bfloat16)
    mixed = reduce_chan(hidden, held_weight, chan_devices, channels)
    return (stream.astype(jnp.float32) + mixed).astype(jnp.bfloat16)


def solution(mesh):
    placed = (
        P("seq"),
        P(None, "chan"),
        P(),
        P(None, None, "chan"),
        P(None, None, "chan"),
        P(None, "chan"),
        P(None, "chan"),
        P("chan"),
        P("chan", None),
    )
    return jax.shard_map(
        on_device, mesh=mesh, in_specs=placed, out_specs=P("seq", "chan"), check_vma=False
    )
```

```python
import jax
import jax.numpy as jnp
from jax import lax
from jax.sharding import PartitionSpec as P

FEAT = 3


def from_behind(value, axis, by):
    devices = lax.axis_size(axis)
    pairs = [(i, i + by) for i in range(devices) if 0 <= i + by < devices]
    return lax.ppermute(value, axis, pairs)


def gather_chan(block, chan_devices):
    ring = chan_devices // 2
    upper = lax.axis_index("chan") >= ring
    where_in_ring = lax.axis_index("chan") % ring

    def along_ring(value, by):
        pairs = [
            (side * ring + z, side * ring + (z + by) % ring)
            for side in range(2)
            for z in range(ring)
        ]
        return lax.ppermute(value, "chan", pairs)

    other = lax.ppermute(block, "chan", [(i, (i + ring) % chan_devices) for i in range(chan_devices)])
    pair = jnp.where(upper, jnp.stack([other, block]), jnp.stack([block, other]))
    ahead, behind = [], []
    fwd, bwd = pair, pair
    for step in range(1, ring // 2 + 1):
        fwd = along_ring(fwd, 1)
        behind.append(fwd)
        if step < ring - ring // 2:
            bwd = along_ring(bwd, -1)
            ahead.append(bwd)
    by_offset = jnp.stack([pair] + ahead + behind[::-1])
    by_place = jnp.roll(by_offset, where_in_ring, axis=0)
    rows = block.shape[0]
    return by_place.transpose(2, 1, 0, 3).reshape(rows, chan_devices * block.shape[1])


def reduce_chan(hidden, out_weight, chan_devices, width):
    ring = chan_devices // 2
    upper = lax.axis_index("chan") >= ring
    where_in_ring = lax.axis_index("chan") % ring
    rows = hidden.shape[0]
    rolled = jnp.roll(
        out_weight.reshape(out_weight.shape[0], 2, ring, width), -where_in_ring, axis=2
    ).reshape(out_weight.shape)
    slabs = jnp.dot(hidden, rolled, preferred_element_type=jnp.float32).reshape(
        rows, 2, ring, width
    )

    def along_ring(value, by):
        pairs = [
            (side * ring + z, side * ring + (z + by) % ring)
            for side in range(2)
            for z in range(ring)
        ]
        return lax.ppermute(value, "chan", pairs)

    pieces = lax.optimization_barrier(tuple(slabs[:, :, o] for o in range(ring)))

    def slab(offset):
        return pieces[offset % ring]

    forward_steps = ring // 2
    backward_steps = ring - 1 - forward_steps
    fwd = slab(forward_steps)
    bwd = slab(-backward_steps)
    for step in range(1, forward_steps + 1):
        fwd = along_ring(fwd.astype(jnp.bfloat16), 1).astype(jnp.float32)
        if step <= backward_steps:
            bwd = along_ring(bwd.astype(jnp.bfloat16), -1).astype(jnp.float32)
        if step < forward_steps:
            fwd = fwd + slab(forward_steps - step)
        if step < backward_steps:
            bwd = bwd + slab(step - backward_steps)
    total = slab(0) + fwd
    if backward_steps > 0:
        total = total + bwd
    mine = jnp.where(upper, total[:, 1], total[:, 0])
    theirs = jnp.where(upper, total[:, 0], total[:, 1])
    partners = [(i, (i + ring) % chan_devices) for i in range(chan_devices)]
    return mine + lax.ppermute(theirs.astype(jnp.bfloat16), "chan", partners).astype(jnp.float32)


def on_device(
    tokens,
    embedding,
    norm_gain,
    in_weight,
    short_filter,
    decay_rate,
    residue,
    skip_gain,
    out_weight,
):
    token_rows = tokens.shape[0]
    vocab_size = embedding.shape[0]
    channels = embedding.shape[1]
    modes = decay_rate.shape[0]
    seq_devices = lax.axis_size("seq")

    one_hot = (tokens[:, None] == jnp.arange(vocab_size, dtype=jnp.int32)[None, :]).astype(
        jnp.bfloat16
    )
    stream = jnp.dot(one_hot, embedding, preferred_element_type=jnp.float32).astype(jnp.bfloat16)
    chan_devices = lax.axis_size("chan")
    gathered = gather_chan(stream, chan_devices)
    gathered_f = gathered.astype(jnp.float32)
    scale = lax.rsqrt(jnp.mean(gathered_f * gathered_f, axis=1, keepdims=True) + 1e-06)
    normed = (gathered_f * scale * norm_gain[None, :]).astype(jnp.bfloat16)
    proj = jnp.einsum("td,djc->tjc", normed, in_weight, preferred_element_type=jnp.float32).astype(
        jnp.bfloat16
    )
    rim_rows = FEAT - 1
    earlier_rim = from_behind(proj[token_rows - rim_rows :], "seq", 1)
    padded = jnp.concatenate([earlier_rim, proj], axis=0).astype(jnp.float32)
    feat = short_filter[0][None] * padded[rim_rows : rim_rows + token_rows]
    for offset in range(1, FEAT):
        feat = (
            feat
            + short_filter[offset][None]
            * padded[rim_rows - offset : rim_rows - offset + token_rows]
        )
    feat = feat.astype(jnp.bfloat16)
    query = feat[:, 0].astype(jnp.float32)
    driven = feat[:, 1].astype(jnp.float32) * feat[:, 2].astype(jnp.float32)

    pos = jnp.arange(token_rows, dtype=jnp.float32)
    rise = jnp.exp(decay_rate[None] * pos[:, None, None])
    fall = residue[None] * jnp.exp(-decay_rate[None] * pos[:, None, None])
    rows = jnp.arange(token_rows)
    lower = (rows[:, None] >= rows[None, :]).astype(jnp.float32)
    lifted = rise * driven[:, None, :]
    running = jnp.dot(
        lower, lifted.reshape(token_rows, modes * channels), precision=lax.Precision.HIGHEST
    ).reshape(token_rows, modes, channels)
    local = jnp.sum(fall * running, axis=1)
    device_end = jnp.exp(-decay_rate * (token_rows - 1)) * jnp.sum(lifted, axis=0)
    held_weight, device_end = lax.optimization_barrier((out_weight, device_end))
    ends = lax.all_to_all(
        jnp.tile(device_end, (seq_devices, 1)), "seq", 0, 0, tiled=True
    ).reshape(seq_devices, modes, channels)
    gap = lax.axis_index("seq") - 1 - jnp.arange(seq_devices)
    span = jnp.exp(
        -decay_rate[None]
        * (token_rows * jnp.maximum(gap, 0)).astype(jnp.float32)[:, None, None]
    )
    span = jnp.where((gap >= 0)[:, None, None], span, 0.0)
    incoming = jnp.sum(span * ends, axis=0) * jnp.exp(-decay_rate)
    carried = jnp.sum(fall * incoming[None], axis=1)
    long_out = local + carried + skip_gain[None, :] * driven
    hidden = (query * long_out).astype(jnp.bfloat16)
    mixed = reduce_chan(hidden, held_weight, chan_devices, channels)
    return (stream.astype(jnp.float32) + mixed).astype(jnp.bfloat16)


def solution(mesh):
    placed = (
        P("seq"),
        P(None, "chan"),
        P(),
        P(None, None, "chan"),
        P(None, None, "chan"),
        P(None, "chan"),
        P(None, "chan"),
        P("chan"),
        P("chan", None),
    )
    return jax.shard_map(
        on_device, mesh=mesh, in_specs=placed, out_specs=P("seq", "chan"), check_vma=False
    )
```

```python
import jax
import jax.numpy as jnp
from jax import lax
from jax.sharding import PartitionSpec as P

FEAT = 3


def from_behind(value, axis, by):
    devices = lax.axis_size(axis)
    pairs = [(i, i + by) for i in range(devices) if 0 <= i + by < devices]
    return lax.ppermute(value, axis, pairs)


def gather_chan(block, chan_devices):
    ring = chan_devices // 2
    upper = lax.axis_index("chan") >= ring
    where_in_ring = lax.axis_index("chan") % ring

    def along_ring(value, by):
        pairs = [
            (side * ring + z, side * ring + (z + by) % ring)
            for side in range(2)
            for z in range(ring)
        ]
        return lax.ppermute(value, "chan", pairs)

    other = lax.ppermute(block, "chan", [(i, (i + ring) % chan_devices) for i in range(chan_devices)])
    pair = jnp.where(upper, jnp.stack([other, block]), jnp.stack([block, other]))
    ahead, behind = [], []
    fwd, bwd = pair, pair
    for step in range(1, ring // 2 + 1):
        fwd = along_ring(fwd, 1)
        behind.append(fwd)
        if step < ring - ring // 2:
            bwd = along_ring(bwd, -1)
            ahead.append(bwd)
    by_offset = jnp.stack([pair] + ahead + behind[::-1])
    by_place = jnp.roll(by_offset, where_in_ring, axis=0)
    rows = block.shape[0]
    return by_place.transpose(2, 1, 0, 3).reshape(rows, chan_devices * block.shape[1])


def reduce_chan(hidden, out_weight, chan_devices, width):
    ring = chan_devices // 2
    upper = lax.axis_index("chan") >= ring
    where_in_ring = lax.axis_index("chan") % ring
    rows = hidden.shape[0]
    rolled = jnp.roll(
        out_weight.reshape(out_weight.shape[0], 2, ring, width), -where_in_ring, axis=2
    ).reshape(out_weight.shape)
    slabs = jnp.dot(hidden, rolled, preferred_element_type=jnp.float32).reshape(
        rows, 2, ring, width
    )

    def along_ring(value, by):
        pairs = [
            (side * ring + z, side * ring + (z + by) % ring)
            for side in range(2)
            for z in range(ring)
        ]
        return lax.ppermute(value, "chan", pairs)

    pieces = lax.optimization_barrier(tuple(slabs[:, :, o] for o in range(ring)))

    def slab(offset):
        return pieces[offset % ring]

    forward_steps = ring // 2
    backward_steps = ring - 1 - forward_steps
    fwd = slab(forward_steps)
    bwd = slab(-backward_steps)
    for step in range(1, forward_steps + 1):
        fwd = along_ring(fwd.astype(jnp.bfloat16), 1).astype(jnp.float32)
        if step <= backward_steps:
            bwd = along_ring(bwd.astype(jnp.bfloat16), -1).astype(jnp.float32)
        if step < forward_steps:
            fwd = fwd + slab(forward_steps - step)
        if step < backward_steps:
            bwd = bwd + slab(step - backward_steps)
    total = slab(0) + fwd
    if backward_steps > 0:
        total = total + bwd
    mine = jnp.where(upper, total[:, 1], total[:, 0])
    theirs = jnp.where(upper, total[:, 0], total[:, 1])
    partners = [(i, (i + ring) % chan_devices) for i in range(chan_devices)]
    return mine + lax.ppermute(theirs.astype(jnp.bfloat16), "chan", partners).astype(jnp.float32)


def on_device(
    tokens,
    embedding,
    norm_gain,
    in_weight,
    short_filter,
    decay_rate,
    residue,
    skip_gain,
    out_weight,
):
    token_rows = tokens.shape[0]
    channels = embedding.shape[1]
    modes = decay_rate.shape[0]
    seq_devices = lax.axis_size("seq")

    stream = jnp.take(embedding, tokens, axis=0, mode="clip")
    chan_devices = lax.axis_size("chan")
    gathered = gather_chan(stream, chan_devices)
    gathered_f = gathered.astype(jnp.float32)
    scale = lax.rsqrt(jnp.mean(gathered_f * gathered_f, axis=1, keepdims=True) + 1e-06)
    normed = (gathered_f * scale * norm_gain[None, :]).astype(jnp.bfloat16)
    proj = jnp.einsum("td,djc->tjc", normed, in_weight, preferred_element_type=jnp.float32).astype(
        jnp.bfloat16
    )
    rim_rows = FEAT - 1
    earlier_rim = from_behind(proj[token_rows - rim_rows :], "seq", 1)
    padded = jnp.concatenate([earlier_rim, proj], axis=0).astype(jnp.float32)
    feat = short_filter[0][None] * padded[rim_rows : rim_rows + token_rows]
    for offset in range(1, FEAT):
        feat = (
            feat
            + short_filter[offset][None]
            * padded[rim_rows - offset : rim_rows - offset + token_rows]
        )
    feat = feat.astype(jnp.bfloat16)
    query = feat[:, 0].astype(jnp.float32)
    driven = feat[:, 1].astype(jnp.float32) * feat[:, 2].astype(jnp.float32)

    pos = jnp.arange(token_rows, dtype=jnp.float32)
    rise = jnp.exp(decay_rate[None] * pos[:, None, None])
    fall = residue[None] * jnp.exp(-decay_rate[None] * pos[:, None, None])
    rows = jnp.arange(token_rows)
    lower = (rows[:, None] >= rows[None, :]).astype(jnp.float32)
    lifted = rise * driven[:, None, :]
    running = jnp.dot(
        lower, lifted.reshape(token_rows, modes * channels), precision=lax.Precision.HIGHEST
    ).reshape(token_rows, modes, channels)
    local = jnp.sum(fall * running, axis=1)
    device_end = jnp.exp(-decay_rate * (token_rows - 1)) * jnp.sum(lifted, axis=0)
    held_weight, device_end = lax.optimization_barrier((out_weight, device_end))
    ends = lax.all_to_all(
        jnp.tile(device_end, (seq_devices, 1)), "seq", 0, 0, tiled=True
    ).reshape(seq_devices, modes, channels)
    gap = lax.axis_index("seq") - 1 - jnp.arange(seq_devices)
    span = jnp.exp(
        -decay_rate[None]
        * (token_rows * jnp.maximum(gap, 0)).astype(jnp.float32)[:, None, None]
    )
    span = jnp.where((gap >= 0)[:, None, None], span, 0.0)
    incoming = jnp.sum(span * ends, axis=0) * jnp.exp(-decay_rate)
    carried = jnp.sum(fall * incoming[None], axis=1)
    long_out = local + carried + skip_gain[None, :] * driven
    hidden = (query * long_out).astype(jnp.bfloat16)
    mixed = reduce_chan(hidden, held_weight, chan_devices, channels)
    return (stream.astype(jnp.float32) + mixed).astype(jnp.bfloat16)


def solution(mesh):
    placed = (
        P("seq"),
        P(None, "chan"),
        P(),
        P(None, None, "chan"),
        P(None, None, "chan"),
        P(None, "chan"),
        P(None, "chan"),
        P("chan"),
        P("chan", None),
    )
    return jax.shard_map(
        on_device, mesh=mesh, in_specs=placed, out_specs=P("seq", "chan"), check_vma=False
    )
```
